128 devices in a mesh: leaf: 4 (over z), panel: 32 (over x, y, core).
Axes of the slice: x: 4, y: 4, z: 4, core: 2. Of those that a mesh axis runs over, the one named last changes fastest.
Arguments:
- right_sides: float32 [4, 1024, 32, 256], P('leaf', 'panel'), may hold values from -6 to 6
- inverse: float32 [4, 1024, 256, 256], P('leaf', 'panel'), as said below
- coupling: float32 [4, 1024, 256, 256], P('leaf', 'panel'), may hold values from -0.25 to 0.25
- owner_map: int32 [4, 1024, 1], P('leaf', 'panel'), may hold values from 0 to 31; in each aligned block of 32 rows (0 to 31, 32 to 63, ..., all dimensions but the last counted through in order) at most 2 rows name the same one
- parent_slot: int32 [4, 1024], P('leaf', 'panel'), may hold values from 0 to 31
Outputs:
- forward_solution: float32 [4, 1024, 32, 256], P('leaf', 'panel')
- backward_solution: float32 [4, 1024, 32, 256], P('leaf', 'panel')
The draws below stay inside these ranges and needn't reach their ends.
Inputs may be any that keep to these rules, and one draw needn't show every extreme that they name: `owner_map`: within the 32 supernodes of one device no owner is named more than 2 times, and some owner is named exactly that often; entries of the top level are not read. `inverse`: each block is upper triangular with a positive diagonal.
All inputs are finite; a program needn't handle non-finite values.
Results may differ from the reference program's by a relative error of at most 0.0001.
Values sent between devices are 32-bit elements; how exact they have to be, the bound alone decides.
No kernel may reach another device: no remote copies, remote signals or barrier semaphores. Data moves between devices by JAX's collectives and lax.ppermute only.
A program may use at most 128 MiB of HBM per device.

```python
import math
import jax
import jax.numpy as jnp
import numpy as np
from jax import lax

BLOCK = 256
RHS_COLS = 32
NODE_DEV = 32
LEVELS = 4
NODES = 1024
CAPACITY = 2
N_PANEL = 32


def draw_inverse(key, part):
    first_key, second_key = jax.random.split(jax.random.fold_in(key, 17))
    shape = (LEVELS, NODES, BLOCK, BLOCK)
    row_index = lax.broadcasted_iota(jnp.int32, (BLOCK, BLOCK), 0)
    col_index = lax.broadcasted_iota(jnp.int32, (BLOCK, BLOCK), 1)
    diagonal = jax.random.uniform(first_key, shape, jnp.float32, 0.6, 1.6)
    above = jax.random.normal(second_key, shape, jnp.float32) * (0.5 / math.sqrt(BLOCK))
    return jnp.where(row_index == col_index, diagonal, jnp.where(col_index > row_index, above, 0.0)).astype(jnp.float32)


def plant(entries, key, low, top_value):
    longest = entries.shape.index(max(entries.shape))
    spots = []
    for shift in (0, 1):
        where = [jax.random.randint(jax.random.fold_in(key, axis), (), 0, length) for axis, length in enumerate(entries.shape)]
        where[longest] = (where[longest] + shift) % entries.shape[longest]
        spots.append(tuple(where))
    return entries.at[spots[0]].set(low).at[spots[1]].set(top_value)


def block_levels(key, extent, pieces, smallest, top_value):
    loudness = 1.0
    for axis_at, parts in pieces:
        heights = jax.random.uniform(jax.random.fold_in(jax.random.fold_in(key, 6), axis_at), (parts,), jnp.float32, smallest / len(pieces), top_value / len(pieces))
        loudness = loudness * jnp.repeat(jnp.exp(heights), extent[axis_at] // parts).reshape((-1,) + (1,) * (len(extent) - 1 - axis_at))
    return loudness


def shared_out(own_key, own, number, rows, number_of, top, limit, skew):
    order = jax.random.permutation(own_key, number_of)
    packed, ordinary = load_shares(number_of, rows * top, limit, skew, True), load_shares(number_of, rows * top, limit, skew, False)
    places = jnp.arange(number_of)

    def named(lengths, rotation):
        used = int((lengths > 0).sum())
        fixed = max(1, used // 4)
        passed = fixed + (places - fixed + rotation * (used - fixed)) % max(1, number_of - fixed)
        return jnp.zeros((number_of,), jnp.int32).at[order[jnp.where(places < fixed, places, passed)]].set(jnp.asarray(lengths, jnp.int32))

    lengths = jnp.where(number % 4 == 0, named(packed, number // 4), named(ordinary, number - number // 4 - 1))
    mixed = jax.random.permutation(jax.random.fold_in(own, 3), number_of)
    giver, sink = mixed[0:number_of // 2 * 2:2], mixed[1:number_of // 2 * 2:2]
    room = jnp.minimum(lengths[giver] - 1, limit - lengths[sink]) // 2
    room = jnp.where((giver == order[0]) | (sink == order[0]) | (lengths[sink] == 0), 0, jnp.maximum(room, 0))
    passed = jax.random.randint(jax.random.fold_in(own, 4), (number_of // 2,), 0, 1 << 20) % (room + 1)
    lengths = lengths.at[giver].add(-passed).at[sink].add(passed)
    labels = jnp.searchsorted(jnp.cumsum(lengths), jnp.arange(rows * top), side="right").astype(jnp.int32)
    grid = labels.reshape(top, rows).T
    grid = grid[jax.random.permutation(jax.random.fold_in(own, 1), rows)]
    rotation = jax.random.randint(jax.random.fold_in(own, 2), (rows, 1), 0, top)
    return jnp.take_along_axis(grid, (jnp.arange(top)[None, :] + rotation) % top, axis=1)


def load_shares(amount, total, reach, slope, full):
    portions = [(1 << 20) // math.isqrt(grade ** slope) + 1 for grade in range(1, amount + 1)]
    largest = reach if full else min(reach, max(-(-total // amount), total * portions[0] // sum(portions)))
    least = 1 if total - largest >= amount - 1 else 0
    holding, surplus = [largest] + [least] * (amount - 1), total - largest - least * (amount - 1)
    while surplus > 0:
        free = [i for i in range(1, amount) if holding[i] < largest] or [i for i in range(1, amount) if holding[i] < reach]
        whole, left = sum([portions[i] for i in free]), surplus
        for i in free:
            addition = min(reach - holding[i], max(1, left * portions[i] // whole), surplus)
            holding[i] = holding[i] + addition
            surplus = surplus - addition
    return np.array(holding)


def centred(own_key, shape, spread, most, cuts=(), dtype=jnp.bfloat16):
    level = block_levels(own_key, shape, cuts, -0.22, 0.18) if cuts else 1.0
    drawn = jax.random.normal(own_key, shape, jnp.float32) * spread * level
    return jnp.minimum(jnp.maximum(drawn, -most), most).astype(dtype)


def setup_inputs(seed: int = 0) -> dict:
    seeds = jax.random.split(jax.random.key(seed), 6)
    right_sides = centred(seeds[0], (LEVELS, NODES, RHS_COLS, BLOCK), 1.0, 6.0, ((0, 4), (1, 32)), jnp.float32)
    inverse = draw_inverse(jax.random.fold_in(seeds[5], 71), 0)
    coupling = centred(seeds[2], (LEVELS, NODES, BLOCK, BLOCK), (2 * BLOCK) ** -0.5, 0.25, ((0, 4), (1, 32)), jnp.float32)
    owner_map_keys = jax.random.split(jax.random.fold_in(seeds[3], 1), LEVELS * NODES // NODE_DEV)
    owner_map_turns = jax.random.permutation(jax.random.fold_in(seeds[3], 3), LEVELS * NODES // NODE_DEV)
    owner_map = jax.vmap(lambda own, number: shared_out(jax.random.fold_in(seeds[3], 2), own, number, NODE_DEV, N_PANEL, 1, CAPACITY, 2))(owner_map_keys, owner_map_turns).reshape((LEVELS, NODES, 1))
    parent_slot = plant(jax.random.randint(seeds[4], (LEVELS, NODES), 0, NODE_DEV), jax.random.fold_in(seeds[4], 1), 0, NODE_DEV - 1).astype(jnp.int32)
    return dict(right_sides=right_sides, inverse=inverse, coupling=coupling, owner_map=owner_map, parent_slot=parent_slot)


def reference(right_sides, inverse, coupling, owner_map, parent_slot):
    highest = lax.Precision.HIGHEST
    parent = (owner_map[:, :, 0] * NODE_DEV + parent_slot).astype(jnp.int32)
    incoming = jnp.zeros(right_sides.shape[1:], jnp.float32)
    forward_list = []
    for level in range(LEVELS):
        solved = jnp.einsum('nrw,nwv->nrv', right_sides[level] - incoming, inverse[level], precision=highest)
        forward_list.append(solved)
        if level < LEVELS - 1:
            updates = jnp.einsum('nrw,nwv->nrv', solved, coupling[level], precision=highest)
            incoming = jax.ops.segment_sum(updates, parent[level], num_segments=NODES)
    backward_list = [None] * LEVELS
    above = jnp.einsum('nrw,nvw->nrv', forward_list[LEVELS - 1], inverse[LEVELS - 1], precision=highest)
    backward_list[LEVELS - 1] = above
    for level in range(LEVELS - 2, -1, -1):
        from_parent = above[parent[level]]
        lowered = jnp.einsum('nrv,nwv->nrw', from_parent, coupling[level], precision=highest)
        above = jnp.einsum('nrw,nvw->nrv', forward_list[level] - lowered, inverse[level], precision=highest)
        backward_list[level] = above
    return jnp.stack(forward_list), jnp.stack(backward_list)
```

```python
import jax
import jax.numpy as jnp
from jax import lax
from jax.sharding import PartitionSpec as P

CHUNKS = 1
MAIN_PRECISION = lax.Precision.HIGHEST


def shift_leaf(block, pairs):
    if not pairs:
        return jnp.zeros_like(block)
    return lax.ppermute(block, "leaf", pairs)


def pick_chunk(chunks, index):
    out = chunks[0]
    for j in range(1, len(chunks)):
        out = jnp.where(index == j, chunks[j], out)
    return out


def store_chunk(chunks, index, piece):
    return [jnp.where(index == j, piece, c) for j, c in enumerate(chunks)]


def body(right_sides, inverse, coupling, owner_map, parent_slot):
    highest = lax.Precision.HIGHEST
    main = MAIN_PRECISION
    levels = lax.axis_size("leaf")
    panels = lax.axis_size("panel")
    level = lax.axis_index("leaf")
    node_count = right_sides.shape[1]
    total_cols = right_sides.shape[2]
    width = right_sides.shape[3]
    capacity = max(2, 2 * node_count // panels)
    slot_count = panels * capacity
    owners = owner_map[0, :, 0]
    positions = parent_slot[0]
    node_iota = jnp.arange(node_count, dtype=jnp.int32)
    same_owner = owners[:, None] == owners[None, :]
    before = node_iota[None, :] < node_iota[:, None]
    slot_rank = jnp.sum((same_owner & before).astype(jnp.int32), axis=1)
    dest_slot = owners * capacity + slot_rank
    slot_iota = jnp.arange(slot_count, dtype=jnp.int32)
    send_onehot = (slot_iota[:, None] == dest_slot[None, :]).astype(jnp.float32)
    send_ids = jnp.dot(send_onehot, (positions + 1).astype(jnp.float32), precision=highest) - 1.0
    arrived_ids = lax.all_to_all(send_ids, "panel", split_axis=0, concat_axis=0, tiled=True)
    node_float = node_iota.astype(jnp.float32)
    recv_onehot = (arrived_ids[None, :] == node_float[:, None]).astype(jnp.float32)

    chunks = CHUNKS
    rows = total_cols // chunks
    given = [right_sides[0, :, j * rows:(j + 1) * rows] for j in range(chunks)]
    diag_inverse = inverse[0]
    couple_block = coupling[0]
    zero_chunk = jnp.zeros((node_count, rows, width), jnp.float32)
    solved = [zero_chunk] * chunks
    result = [zero_chunk] * chunks
    incoming = zero_chunk
    picked = zero_chunk
    top = levels - 1
    turns = 2 * top + chunks
    for turn in range(turns):
        fwd_levels = [l for l in range(levels) if 0 <= turn - l < chunks]
        bwd_levels = [l for l in range(levels) if 0 <= turn - 2 * top + l < chunks]
        if fwd_levels:
            f_index = turn - level
            f_active = (f_index >= 0) & (f_index < chunks)
            rhs = pick_chunk(given, f_index)
            forward_part = jnp.einsum("nrw,nwv->nrv", rhs - incoming, diag_inverse, precision=main)
            solved = store_chunk(solved, jnp.where(f_active, f_index, -1), forward_part)
        if bwd_levels:
            b_index = turn - 2 * top + level
            b_active = (b_index >= 0) & (b_index < chunks)
            source = pick_chunk(solved, b_index)
            if any(l < top for l in bwd_levels):
                lowered = jnp.einsum("nrv,nwv->nrw", picked, couple_block, precision=main)
                source = source - lowered
            backward_part = jnp.einsum("nrw,nvw->nrv", source, diag_inverse, precision=main)
            result = store_chunk(result, jnp.where(b_active, b_index, -1), backward_part)
        senders = [l for l in fwd_levels if l < top]
        if senders:
            updates = jnp.einsum("nrw,nwv->nrv", forward_part, couple_block, precision=main)
            buffer = jnp.einsum("ts,srw->trw", send_onehot, updates, precision=highest)
            arrived = lax.all_to_all(buffer, "panel", split_axis=0, concat_axis=0, tiled=True)
            summed = jnp.einsum("st,trw->srw", recv_onehot, arrived, precision=highest)
            incoming = shift_leaf(summed, [(l, l + 1) for l in senders])
        else:
            incoming = zero_chunk
        down = [l for l in bwd_levels if l > 0]
        if down:
            lowered_in = shift_leaf(backward_part, [(l, l - 1) for l in down])
            buffer = jnp.einsum("st,srw->trw", recv_onehot, lowered_in, precision=highest)
            arrived = lax.all_to_all(buffer, "panel", split_axis=0, concat_axis=0, tiled=True)
            picked = jnp.einsum("ts,trw->srw", send_onehot, arrived, precision=highest)
        else:
            picked = zero_chunk
    solved_all = jnp.concatenate(solved, axis=1)
    result_all = jnp.concatenate(result, axis=1)
    return (solved_all[None], result_all[None])


def solution(mesh):
    in_specs = (
        P("leaf", "panel", None, None),
        P("leaf", "panel", None, None),
        P("leaf", "panel", None, None),
        P("leaf", "panel", None),
        P("leaf", "panel"),
    )
    out_specs = (P("leaf", "panel", None, None), P("leaf", "panel", None, None))
    return jax.shard_map(body, mesh=mesh, in_specs=in_specs, out_specs=out_specs, check_vma=False)
```

```python
import jax
import jax.numpy as jnp
from jax import lax
from jax.sharding import PartitionSpec as P

CHUNKS = 2
MAIN_PRECISION = lax.Precision.HIGHEST


def shift_leaf(block, pairs):
    if not pairs:
        return jnp.zeros_like(block)
    return lax.ppermute(block, "leaf", pairs)


def pick_chunk(chunks, index):
    out = chunks[0]
    for j in range(1, len(chunks)):
        out = jnp.where(index == j, chunks[j], out)
    return out


def store_chunk(chunks, index, piece):
    return [jnp.where(index == j, piece, c) for j, c in enumerate(chunks)]


def body(right_sides, inverse, coupling, owner_map, parent_slot):
    highest = lax.Precision.HIGHEST
    main = MAIN_PRECISION
    levels = lax.axis_size("leaf")
    panels = lax.axis_size("panel")
    level = lax.axis_index("leaf")
    node_count = right_sides.shape[1]
    total_cols = right_sides.shape[2]
    width = right_sides.shape[3]
    capacity = max(2, 2 * node_count // panels)
    slot_count = panels * capacity
    owners = owner_map[0, :, 0]
    positions = parent_slot[0]
    node_iota = jnp.arange(node_count, dtype=jnp.int32)
    same_owner = owners[:, None] == owners[None, :]
    before = node_iota[None, :] < node_iota[:, None]
    slot_rank = jnp.sum((same_owner & before).astype(jnp.int32), axis=1)
    dest_slot = owners * capacity + slot_rank
    slot_iota = jnp.arange(slot_count, dtype=jnp.int32)
    send_onehot = (slot_iota[:, None] == dest_slot[None, :]).astype(jnp.float32)
    send_ids = jnp.dot(send_onehot, (positions + 1).astype(jnp.float32), precision=highest) - 1.0
    arrived_ids = lax.all_to_all(send_ids, "panel", split_axis=0, concat_axis=0, tiled=True)
    node_float = node_iota.astype(jnp.float32)
    recv_onehot = (arrived_ids[None, :] == node_float[:, None]).astype(jnp.float32)

    chunks = CHUNKS
    rows = total_cols // chunks
    given = [right_sides[0, :, j * rows:(j + 1) * rows] for j in range(chunks)]
    diag_inverse = inverse[0]
    couple_block = coupling[0]
    zero_chunk = jnp.zeros((node_count, rows, width), jnp.float32)
    solved = [zero_chunk] * chunks
    result = [zero_chunk] * chunks
    incoming = zero_chunk
    picked = zero_chunk
    top = levels - 1
    turns = 2 * top + chunks
    for turn in range(turns):
        fwd_levels = [l for l in range(levels) if 0 <= turn - l < chunks]
        bwd_levels = [l for l in range(levels) if 0 <= turn - 2 * top + l < chunks]
        if fwd_levels:
            f_index = turn - level
            f_active = (f_index >= 0) & (f_index < chunks)
            rhs = pick_chunk(given, f_index)
            forward_part = jnp.einsum("nrw,nwv->nrv", rhs - incoming, diag_inverse, precision=main)
            solved = store_chunk(solved, jnp.where(f_active, f_index, -1), forward_part)
        if bwd_levels:
            b_index = turn - 2 * top + level
            b_active = (b_index >= 0) & (b_index < chunks)
            source = pick_chunk(solved, b_index)
            if any(l < top for l in bwd_levels):
                lowered = jnp.einsum("nrv,nwv->nrw", picked, couple_block, precision=main)
                source = source - lowered
            backward_part = jnp.einsum("nrw,nvw->nrv", source, diag_inverse, precision=main)
            result = store_chunk(result, jnp.where(b_active, b_index, -1), backward_part)
        senders = [l for l in fwd_levels if l < top]
        if senders:
            updates = jnp.einsum("nrw,nwv->nrv", forward_part, couple_block, precision=main)
            buffer = jnp.einsum("ts,srw->trw", send_onehot, updates, precision=highest)
            arrived = lax.all_to_all(buffer, "panel", split_axis=0, concat_axis=0, tiled=True)
            summed = jnp.einsum("st,trw->srw", recv_onehot, arrived, precision=highest)
            incoming = shift_leaf(summed, [(l, l + 1) for l in senders])
        else:
            incoming = zero_chunk
        down = [l for l in bwd_levels if l > 0]
        if down:
            lowered_in = shift_leaf(backward_part, [(l, l - 1) for l in down])
            buffer = jnp.einsum("st,srw->trw", recv_onehot, lowered_in, precision=highest)
            arrived = lax.all_to_all(buffer, "panel", split_axis=0, concat_axis=0, tiled=True)
            picked = jnp.einsum("ts,trw->srw", send_onehot, arrived, precision=highest)
        else:
            picked = zero_chunk
    solved_all = jnp.concatenate(solved, axis=1)
    result_all = jnp.concatenate(result, axis=1)
    return (solved_all[None], result_all[None])


def solution(mesh):
    in_specs = (
        P("leaf", "panel", None, None),
        P("leaf", "panel", None, None),
        P("leaf", "panel", None, None),
        P("leaf", "panel", None),
        P("leaf", "panel"),
    )
    out_specs = (P("leaf", "panel", None, None), P("leaf", "panel", None, None))
    return jax.shard_map(body, mesh=mesh, in_specs=in_specs, out_specs=out_specs, check_vma=False)
```

```python
import jax
import jax.numpy as jnp
from jax import lax
from jax.sharding import PartitionSpec as P

CHUNKS = 2
MAIN_PRECISION = lax.Precision.HIGH


def shift_leaf(block, pairs):
    if not pairs:
        return jnp.zeros_like(block)
    return lax.ppermute(block, "leaf", pairs)


def pick_chunk(chunks, index):
    out = chunks[0]
    for j in range(1, len(chunks)):
        out = jnp.where(index == j, chunks[j], out)
    return out


def store_chunk(chunks, index, piece):
    return [jnp.where(index == j, piece, c) for j, c in enumerate(chunks)]


def body(right_sides, inverse, coupling, owner_map, parent_slot):
    highest = lax.Precision.HIGHEST
    main = MAIN_PRECISION
    levels = lax.axis_size("leaf")
    panels = lax.axis_size("panel")
    level = lax.axis_index("leaf")
    node_count = right_sides.shape[1]
    total_cols = right_sides.shape[2]
    width = right_sides.shape[3]
    capacity = max(2, 2 * node_count // panels)
    slot_count = panels * capacity
    owners = owner_map[0, :, 0]
    positions = parent_slot[0]
    node_iota = jnp.arange(node_count, dtype=jnp.int32)
    same_owner = owners[:, None] == owners[None, :]
    before = node_iota[None, :] < node_iota[:, None]
    slot_rank = jnp.sum((same_owner & before).astype(jnp.int32), axis=1)
    dest_slot = owners * capacity + slot_rank
    slot_iota = jnp.arange(slot_count, dtype=jnp.int32)
    send_onehot = (slot_iota[:, None] == dest_slot[None, :]).astype(jnp.float32)
    send_ids = jnp.dot(send_onehot, (positions + 1).astype(jnp.float32), precision=highest) - 1.0
    arrived_ids = lax.all_to_all(send_ids, "panel", split_axis=0, concat_axis=0, tiled=True)
    node_float = node_iota.astype(jnp.float32)
    recv_onehot = (arrived_ids[None, :] == node_float[:, None]).astype(jnp.float32)

    chunks = CHUNKS
    rows = total_cols // chunks
    given = [right_sides[0, :, j * rows:(j + 1) * rows] for j in range(chunks)]
    diag_inverse = inverse[0]
    couple_block = coupling[0]
    zero_chunk = jnp.zeros((node_count, rows, width), jnp.float32)
    solved = [zero_chunk] * chunks
    result = [zero_chunk] * chunks
    incoming = zero_chunk
    picked = zero_chunk
    top = levels - 1
    turns = 2 * top + chunks
    for turn in range(turns):
        fwd_levels = [l for l in range(levels) if 0 <= turn - l < chunks]
        bwd_levels = [l for l in range(levels) if 0 <= turn - 2 * top + l < chunks]
        if fwd_levels:
            f_index = turn - level
            f_active = (f_index >= 0) & (f_index < chunks)
            rhs = pick_chunk(given, f_index)
            forward_part = jnp.einsum("nrw,nwv->nrv", rhs - incoming, diag_inverse, precision=main)
            solved = store_chunk(solved, jnp.where(f_active, f_index, -1), forward_part)
        if bwd_levels:
            b_index = turn - 2 * top + level
            b_active = (b_index >= 0) & (b_index < chunks)
            source = pick_chunk(solved, b_index)
            if any(l < top for l in bwd_levels):
                lowered = jnp.einsum("nrv,nwv->nrw", picked, couple_block, precision=main)
                source = source - lowered
            backward_part = jnp.einsum("nrw,nvw->nrv", source, diag_inverse, precision=main)
            result = store_chunk(result, jnp.where(b_active, b_index, -1), backward_part)
        senders = [l for l in fwd_levels if l < top]
        if senders:
            updates = jnp.einsum("nrw,nwv->nrv", forward_part, couple_block, precision=main)
            buffer = jnp.einsum("ts,srw->trw", send_onehot, updates, precision=highest)
            arrived = lax.all_to_all(buffer, "panel", split_axis=0, concat_axis=0, tiled=True)
            summed = jnp.einsum("st,trw->srw", recv_onehot, arrived, precision=highest)
            incoming = shift_leaf(summed, [(l, l + 1) for l in senders])
        else:
            incoming = zero_chunk
        down = [l for l in bwd_levels if l > 0]
        if down:
            lowered_in = shift_leaf(backward_part, [(l, l - 1) for l in down])
            buffer = jnp.einsum("st,srw->trw", recv_onehot, lowered_in, precision=highest)
            arrived = lax.all_to_all(buffer, "panel", split_axis=0, concat_axis=0, tiled=True)
            picked = jnp.einsum("ts,trw->srw", send_onehot, arrived, precision=highest)
        else:
            picked = zero_chunk
    solved_all = jnp.concatenate(solved, axis=1)
    result_all = jnp.concatenate(result, axis=1)
    return (solved_all[None], result_all[None])


def solution(mesh):
    in_specs = (
        P("leaf", "panel", None, None),
        P("leaf", "panel", None, None),
        P("leaf", "panel", None, None),
        P("leaf", "panel", None),
        P("leaf", "panel"),
    )
    out_specs = (P("leaf", "panel", None, None), P("leaf", "panel", None, None))
    return jax.shard_map(body, mesh=mesh, in_specs=in_specs, out_specs=out_specs, check_vma=False)
```

```python
import jax
import jax.numpy as jnp
from jax import lax
from jax.sharding import PartitionSpec as P

MAIN_PRECISION = lax.Precision.HIGHEST


def shift_leaf(block, pairs):
    return lax.ppermute(block, "leaf", pairs)


def exchange(buffer):
    return lax.all_to_all(buffer, "panel", split_axis=0, concat_axis=0, tiled=True)


def body(right_sides, inverse, coupling, owner_map, parent_slot):
    highest = lax.Precision.HIGHEST
    main = MAIN_PRECISION
    levels = lax.axis_size("leaf")
    panels = lax.axis_size("panel")
    level = lax.axis_index("leaf")
    node_count = right_sides.shape[1]
    total_cols = right_sides.shape[2]
    capacity = max(2, 2 * node_count // panels)
    slot_count = panels * capacity
    owners = owner_map[0, :, 0]
    positions = parent_slot[0]
    node_iota = jnp.arange(node_count, dtype=jnp.int32)
    same_owner = owners[:, None] == owners[None, :]
    before = node_iota[None, :] < node_iota[:, None]
    slot_rank = jnp.sum((same_owner & before).astype(jnp.int32), axis=1)
    dest_slot = owners * capacity + slot_rank
    slot_iota = jnp.arange(slot_count, dtype=jnp.int32)
    send_onehot = (slot_iota[:, None] == dest_slot[None, :]).astype(jnp.float32)
    send_ids = jnp.dot(send_onehot, (positions + 1).astype(jnp.float32), precision=highest) - 1.0
    arrived_ids = exchange(send_ids)
    node_float = node_iota.astype(jnp.float32)
    recv_onehot = (arrived_ids[None, :] == node_float[:, None]).astype(jnp.float32)
    up_pairs = [(l, l + 1) for l in range(levels - 1)]
    send_below, recv_below = shift_leaf((send_onehot, recv_onehot), up_pairs)

    half = total_cols // 2
    given = right_sides[0]
    diag_inverse = inverse[0]
    couple_block = coupling[0]
    top = levels - 1
    incoming = jnp.zeros_like(given)
    solved = None
    for turn in range(levels):
        part = jnp.einsum("nrw,nwv->nrv", given - incoming, diag_inverse, precision=main)
        solved = part if solved is None else jnp.where(level == turn, part, solved)
        if turn < top:
            pairs = [(turn, turn + 1)]
            updates = jnp.einsum("nrw,nwv->nrv", part, couple_block, precision=main)
            raw_up = shift_leaf(updates[:, half:], pairs)
            arrived = exchange(jnp.einsum("ts,srw->trw", send_onehot, updates[:, :half], precision=highest))
            summed = jnp.einsum("st,trw->srw", recv_onehot, arrived, precision=highest)
            first = shift_leaf(summed, pairs)
            arrived = exchange(jnp.einsum("ts,srw->trw", send_below, raw_up, precision=highest))
            second = jnp.einsum("st,trw->srw", recv_below, arrived, precision=highest)
            incoming = jnp.concatenate([first, second], axis=1)
    result = None
    picked = None
    for upper in range(top, -1, -1):
        source = solved
        if picked is not None:
            source = source - jnp.einsum("nrv,nwv->nrw", picked, couple_block, precision=main)
        part = jnp.einsum("nrw,nvw->nrv", source, diag_inverse, precision=main)
        result = part if result is None else jnp.where(level == upper, part, result)
        if upper > 0:
            pairs = [(upper, upper - 1)]
            low = shift_leaf(part[:, :half], pairs)
            arrived = exchange(jnp.einsum("st,srw->trw", recv_below, part[:, half:], precision=highest))
            raw_down = jnp.einsum("ts,trw->srw", send_below, arrived, precision=highest)
            arrived = exchange(jnp.einsum("st,srw->trw", recv_onehot, low, precision=highest))
            first = jnp.einsum("ts,trw->srw", send_onehot, arrived, precision=highest)
            second = shift_leaf(raw_down, pairs)
            picked = jnp.concatenate([first, second], axis=1)
    return (solved[None], result[None])


def solution(mesh):
    in_specs = (
        P("leaf", "panel", None, None),
        P("leaf", "panel", None, None),
        P("leaf", "panel", None, None),
        P("leaf", "panel", None),
        P("leaf", "panel"),
    )
    out_specs = (P("leaf", "panel", None, None), P("leaf", "panel", None, None))
    return jax.shard_map(body, mesh=mesh, in_specs=in_specs, out_specs=out_specs, check_vma=False)
```

```python
import jax
import jax.numpy as jnp
from jax import lax
from jax.sharding import PartitionSpec as P
from jax.experimental.layout import Layout, with_layout_constraint

CHUNKS = 2
MAIN_PRECISION = lax.Precision.HIGHEST


def shift_leaf(block, pairs):
    if not pairs:
        return jnp.zeros_like(block)
    return lax.ppermute(block, "leaf", pairs)


def pick_chunk(chunks, index):
    out = chunks[0]
    for j in range(1, len(chunks)):
        out = jnp.where(index == j, chunks[j], out)
    return out


def store_chunk(chunks, index, piece):
    return [jnp.where(index == j, piece, c) for j, c in enumerate(chunks)]


def body(right_sides, inverse, coupling, owner_map, parent_slot):
    highest = lax.Precision.HIGHEST
    main = MAIN_PRECISION
    levels = lax.axis_size("leaf")
    panels = lax.axis_size("panel")
    level = lax.axis_index("leaf")
    node_count = right_sides.shape[1]
    total_cols = right_sides.shape[2]
    width = right_sides.shape[3]
    capacity = max(2, 2 * node_count // panels)
    slot_count = panels * capacity
    owners = owner_map[0, :, 0]
    positions = parent_slot[0]
    node_iota = jnp.arange(node_count, dtype=jnp.int32)
    same_owner = owners[:, None] == owners[None, :]
    before = node_iota[None, :] < node_iota[:, None]
    slot_rank = jnp.sum((same_owner & before).astype(jnp.int32), axis=1)
    dest_slot = owners * capacity + slot_rank
    slot_iota = jnp.arange(slot_count, dtype=jnp.int32)
    send_onehot = (slot_iota[:, None] == dest_slot[None, :]).astype(jnp.float32)
    send_ids = jnp.dot(send_onehot, (positions + 1).astype(jnp.float32), precision=highest) - 1.0
    arrived_ids = lax.all_to_all(send_ids, "panel", split_axis=0, concat_axis=0, tiled=True)
    node_float = node_iota.astype(jnp.float32)
    recv_onehot = (arrived_ids[None, :] == node_float[:, None]).astype(jnp.float32)

    chunks = CHUNKS
    rows = total_cols // chunks
    given = [right_sides[0, :, j * rows:(j + 1) * rows] for j in range(chunks)]
    diag_inverse = inverse[0]
    couple_block = coupling[0]
    row_major = Layout(major_to_minor=(0, 1, 2))
    inverse_t = with_layout_constraint(jnp.swapaxes(diag_inverse, 1, 2), row_major)
    couple_t = with_layout_constraint(jnp.swapaxes(couple_block, 1, 2), row_major)
    zero_chunk = jnp.zeros((node_count, rows, width), jnp.float32)
    solved = [zero_chunk] * chunks
    result = [zero_chunk] * chunks
    incoming = zero_chunk
    picked = zero_chunk
    top = levels - 1
    turns = 2 * top + chunks
    for turn in range(turns):
        fwd_levels = [l for l in range(levels) if 0 <= turn - l < chunks]
        bwd_levels = [l for l in range(levels) if 0 <= turn - 2 * top + l < chunks]
        if fwd_levels:
            f_index = turn - level
            f_active = (f_index >= 0) & (f_index < chunks)
            rhs = pick_chunk(given, f_index)
            forward_part = jnp.einsum("nrw,nwv->nrv", rhs - incoming, diag_inverse, precision=main)
            solved = store_chunk(solved, jnp.where(f_active, f_index, -1), forward_part)
        if bwd_levels:
            b_index = turn - 2 * top + level
            b_active = (b_index >= 0) & (b_index < chunks)
            source = pick_chunk(solved, b_index)
            if any(l < top for l in bwd_levels):
                lowered = jnp.einsum("nrv,nvw->nrw", picked, couple_t, precision=main)
                source = source - lowered
            backward_part = jnp.einsum("nrw,nwv->nrv", source, inverse_t, precision=main)
            result = store_chunk(result, jnp.where(b_active, b_index, -1), backward_part)
        senders = [l for l in fwd_levels if l < top]
        if senders:
            updates = jnp.einsum("nrw,nwv->nrv", forward_part, couple_block, precision=main)
            buffer = jnp.einsum("ts,srw->trw", send_onehot, updates, precision=highest)
            arrived = lax.all_to_all(buffer, "panel", split_axis=0, concat_axis=0, tiled=True)
            summed = jnp.einsum("st,trw->srw", recv_onehot, arrived, precision=highest)
            incoming = shift_leaf(summed, [(l, l + 1) for l in senders])
        else:
            incoming = zero_chunk
        down = [l for l in bwd_levels if l > 0]
        if down:
            lowered_in = shift_leaf(backward_part, [(l, l - 1) for l in down])
            buffer = jnp.einsum("st,srw->trw", recv_onehot, lowered_in, precision=highest)
            arrived = lax.all_to_all(buffer, "panel", split_axis=0, concat_axis=0, tiled=True)
            picked = jnp.einsum("ts,trw->srw", send_onehot, arrived, precision=highest)
        else:
            picked = zero_chunk
    solved_all = jnp.concatenate(solved, axis=1)
    result_all = jnp.concatenate(result, axis=1)
    return (solved_all[None], result_all[None])


def solution(mesh):
    in_specs = (
        P("leaf", "panel", None, None),
        P("leaf", "panel", None, None),
        P("leaf", "panel", None, None),
        P("leaf", "panel", None),
        P("leaf", "panel"),
    )
    out_specs = (P("leaf", "panel", None, None), P("leaf", "panel", None, None))
    return jax.shard_map(body, mesh=mesh, in_specs=in_specs, out_specs=out_specs, check_vma=False)
```

```python
import jax
import jax.numpy as jnp
from jax import lax
from jax.sharding import PartitionSpec as P
from jax.experimental.layout import Layout, with_layout_constraint

CHUNKS = 4
MAIN_PRECISION = lax.Precision.HIGHEST


def shift_leaf(block, pairs):
    return lax.ppermute(block, "leaf", pairs)


def exchange(buffer):
    return lax.all_to_all(buffer, "panel", split_axis=0, concat_axis=0, tiled=True)


def pick_chunk(chunks, index):
    out = chunks[0]
    for j in range(1, len(chunks)):
        out = jnp.where(index == j, chunks[j], out)
    return out


def store_chunk(chunks, index, piece):
    return [jnp.where(index == j, piece, c) for j, c in enumerate(chunks)]


def body(right_sides, inverse, coupling, owner_map, parent_slot):
    highest = lax.Precision.HIGHEST
    main = MAIN_PRECISION
    levels = lax.axis_size("leaf")
    panels = lax.axis_size("panel")
    level = lax.axis_index("leaf")
    node_count = right_sides.shape[1]
    total_cols = right_sides.shape[2]
    width = right_sides.shape[3]
    capacity = max(2, 2 * node_count // panels)
    slot_count = panels * capacity
    owners = owner_map[0, :, 0]
    positions = parent_slot[0]
    node_iota = jnp.arange(node_count, dtype=jnp.int32)
    same_owner = owners[:, None] == owners[None, :]
    before = node_iota[None, :] < node_iota[:, None]
    slot_rank = jnp.sum((same_owner & before).astype(jnp.int32), axis=1)
    dest_slot = owners * capacity + slot_rank
    slot_iota = jnp.arange(slot_count, dtype=jnp.int32)
    send_onehot = (slot_iota[:, None] == dest_slot[None, :]).astype(jnp.float32)
    send_ids = jnp.dot(send_onehot, (positions + 1).astype(jnp.float32), precision=highest) - 1.0
    arrived_ids = exchange(send_ids)
    node_float = node_iota.astype(jnp.float32)
    recv_onehot = (arrived_ids[None, :] == node_float[:, None]).astype(jnp.float32)

    chunks = CHUNKS
    rows = total_cols // chunks
    given = [right_sides[0, :, j * rows:(j + 1) * rows] for j in range(chunks)]
    diag_inverse = inverse[0]
    couple_block = coupling[0]
    row_major = Layout(major_to_minor=(0, 1, 2))
    inverse_t = with_layout_constraint(jnp.swapaxes(diag_inverse, 1, 2), row_major)
    couple_t = with_layout_constraint(jnp.swapaxes(couple_block, 1, 2), row_major)
    zero_chunk = jnp.zeros((node_count, rows, width), jnp.float32)
    solved = [zero_chunk] * chunks
    result = [zero_chunk] * chunks
    incoming = zero_chunk
    picked = zero_chunk
    top = levels - 1
    turns = 2 * top + chunks
    for turn in range(turns):
        fwd_levels = [l for l in range(levels) if 0 <= turn - l < chunks]
        bwd_levels = [l for l in range(levels) if 0 <= turn - 2 * top + l < chunks]
        if fwd_levels:
            f_index = turn - level
            f_active = (f_index >= 0) & (f_index < chunks)
            rhs = pick_chunk(given, f_index)
            forward_part = jnp.einsum("nrw,nwv->nrv", rhs - incoming, diag_inverse, precision=main)
            solved = store_chunk(solved, jnp.where(f_active, f_index, -1), forward_part)
        if bwd_levels:
            b_index = turn - 2 * top + level
            b_active = (b_index >= 0) & (b_index < chunks)
            source = pick_chunk(solved, b_index)
            if any(l < top for l in bwd_levels):
                lowered = jnp.einsum("nrv,nvw->nrw", picked, couple_t, precision=main)
                source = source - lowered
            backward_part = jnp.einsum("nrw,nwv->nrv", source, inverse_t, precision=main)
            result = store_chunk(result, jnp.where(b_active, b_index, -1), backward_part)
        senders = [l for l in fwd_levels if l < top]
        down = [l for l in bwd_levels if l > 0]
        if senders:
            updates = jnp.einsum("nrw,nwv->nrv", forward_part, couple_block, precision=main)
            fwd_buffer = jnp.einsum("ts,srw->trw", send_onehot, updates, precision=highest)
        if down:
            lowered_in = shift_leaf(backward_part, [(l, l - 1) for l in down])
            bwd_buffer = jnp.einsum("st,srw->trw", recv_onehot, lowered_in, precision=highest)
        if senders and down:
            arrived = exchange(jnp.concatenate([fwd_buffer, bwd_buffer], axis=1))
            fwd_arrived, bwd_arrived = arrived[:, :rows], arrived[:, rows:]
        elif senders:
            fwd_arrived = exchange(fwd_buffer)
        elif down:
            bwd_arrived = exchange(bwd_buffer)
        if senders:
            summed = jnp.einsum("st,trw->srw", recv_onehot, fwd_arrived, precision=highest)
            incoming = shift_leaf(summed, [(l, l + 1) for l in senders])
        else:
            incoming = zero_chunk
        if down:
            picked = jnp.einsum("ts,trw->srw", send_onehot, bwd_arrived, precision=highest)
        else:
            picked = zero_chunk
    solved_all = jnp.concatenate(solved, axis=1)
    result_all = jnp.concatenate(result, axis=1)
    return (solved_all[None], result_all[None])


def solution(mesh):
    in_specs = (
        P("leaf", "panel", None, None),
        P("leaf", "panel", None, None),
        P("leaf", "panel", None, None),
        P("leaf", "panel", None),
        P("leaf", "panel"),
    )
    out_specs = (P("leaf", "panel", None, None), P("leaf", "panel", None, None))
    return jax.shard_map(body, mesh=mesh, in_specs=in_specs, out_specs=out_specs, check_vma=False)
```

```python
import jax
import jax.numpy as jnp
from jax import lax
from jax.sharding import PartitionSpec as P
from jax.experimental.layout import Layout, with_layout_constraint

CHUNKS = 4


def shift_leaf(block, pairs):
    return lax.ppermute(block, "leaf", pairs)


def exchange(buffer):
    return lax.all_to_all(buffer, "panel", split_axis=0, concat_axis=0, tiled=True)


def split3(a):
    rounded = lambda v: lax.reduce_precision(v, exponent_bits=8, mantissa_bits=7)
    hi = rounded(a)
    rest = a - hi
    mid = rounded(rest)
    lo = rest - mid
    return tuple(p.astype(jnp.bfloat16) for p in (hi, mid, lo))


def product(x, parts):
    hi, mid, lo = parts
    rows = x.shape[1]
    xh, xm, xl = split3(x)
    mul = lambda a, w: jnp.einsum("nrw,nwv->nrv", a, w, preferred_element_type=jnp.float32)
    first = mul(jnp.concatenate([xh, xm, xl], axis=1), hi)
    second = mul(jnp.concatenate([xh, xm], axis=1), mid)
    third = mul(xh, lo)
    small = (first[:, 2 * rows:] + second[:, rows:] + third) + (first[:, rows:2 * rows] + second[:, :rows])
    return small + first[:, :rows]


def pick_chunk(chunks, index):
    out = chunks[0]
    for j in range(1, len(chunks)):
        out = jnp.where(index == j, chunks[j], out)
    return out


def store_chunk(chunks, index, piece):
    return [jnp.where(index == j, piece, c) for j, c in enumerate(chunks)]


def body(right_sides, inverse, coupling, owner_map, parent_slot):
    highest = lax.Precision.HIGHEST
    levels = lax.axis_size("leaf")
    panels = lax.axis_size("panel")
    level = lax.axis_index("leaf")
    node_count = right_sides.shape[1]
    total_cols = right_sides.shape[2]
    width = right_sides.shape[3]
    capacity = max(2, 2 * node_count // panels)
    slot_count = panels * capacity
    owners = owner_map[0, :, 0]
    positions = parent_slot[0]
    node_iota = jnp.arange(node_count, dtype=jnp.int32)
    same_owner = owners[:, None] == owners[None, :]
    before = node_iota[None, :] < node_iota[:, None]
    slot_rank = jnp.sum((same_owner & before).astype(jnp.int32), axis=1)
    dest_slot = owners * capacity + slot_rank
    slot_iota = jnp.arange(slot_count, dtype=jnp.int32)
    send_onehot = (slot_iota[:, None] == dest_slot[None, :]).astype(jnp.float32)
    send_ids = jnp.dot(send_onehot, (positions + 1).astype(jnp.float32), precision=highest) - 1.0
    arrived_ids = exchange(send_ids)
    node_float = node_iota.astype(jnp.float32)
    recv_onehot = (arrived_ids[None, :] == node_float[:, None]).astype(jnp.float32)

    chunks = CHUNKS
    rows = total_cols // chunks
    given = [right_sides[0, :, j * rows:(j + 1) * rows] for j in range(chunks)]
    diag_inverse = inverse[0]
    couple_block = coupling[0]
    row_major = Layout(major_to_minor=(0, 1, 2))
    inverse_t = with_layout_constraint(jnp.swapaxes(diag_inverse, 1, 2), row_major)
    couple_t = with_layout_constraint(jnp.swapaxes(couple_block, 1, 2), row_major)
    inverse_parts = split3(diag_inverse)
    couple_parts = split3(couple_block)
    inverse_t_parts = split3(inverse_t)
    couple_t_parts = split3(couple_t)
    zero_chunk = jnp.zeros((node_count, rows, width), jnp.float32)
    solved = [zero_chunk] * chunks
    result = [zero_chunk] * chunks
    incoming = zero_chunk
    picked = zero_chunk
    top = levels - 1
    turns = 2 * top + chunks
    for turn in range(turns):
        fwd_levels = [l for l in range(levels) if 0 <= turn - l < chunks]
        bwd_levels = [l for l in range(levels) if 0 <= turn - 2 * top + l < chunks]
        if fwd_levels:
            f_index = turn - level
            f_active = (f_index >= 0) & (f_index < chunks)
            rhs = pick_chunk(given, f_index)
            forward_part = product(rhs - incoming, inverse_parts)
            solved = store_chunk(solved, jnp.where(f_active, f_index, -1), forward_part)
        if bwd_levels:
            b_index = turn - 2 * top + level
            b_active = (b_index >= 0) & (b_index < chunks)
            source = pick_chunk(solved, b_index)
            if any(l < top for l in bwd_levels):
                lowered = product(picked, couple_t_parts)
                source = source - lowered
            backward_part = product(source, inverse_t_parts)
            result = store_chunk(result, jnp.where(b_active, b_index, -1), backward_part)
        senders = [l for l in fwd_levels if l < top]
        down = [l for l in bwd_levels if l > 0]
        if senders:
            updates = product(forward_part, couple_parts)
            fwd_buffer = jnp.einsum("ts,srw->trw", send_onehot, updates, precision=highest)
        if down:
            lowered_in = shift_leaf(backward_part, [(l, l - 1) for l in down])
            bwd_buffer = jnp.einsum("st,srw->trw", recv_onehot, lowered_in, precision=highest)
        if senders and down:
            arrived = exchange(jnp.concatenate([fwd_buffer, bwd_buffer], axis=1))
            fwd_arrived, bwd_arrived = arrived[:, :rows], arrived[:, rows:]
        elif senders:
            fwd_arrived = exchange(fwd_buffer)
        elif down:
            bwd_arrived = exchange(bwd_buffer)
        if senders:
            summed = jnp.einsum("st,trw->srw", recv_onehot, fwd_arrived, precision=highest)
            incoming = shift_leaf(summed, [(l, l + 1) for l in senders])
        else:
            incoming = zero_chunk
        if down:
            picked = jnp.einsum("ts,trw->srw", send_onehot, bwd_arrived, precision=highest)
        else:
            picked = zero_chunk
    solved_all = jnp.concatenate(solved, axis=1)
    result_all = jnp.concatenate(result, axis=1)
    return (solved_all[None], result_all[None])


def solution(mesh):
    in_specs = (
        P("leaf", "panel", None, None),
        P("leaf", "panel", None, None),
        P("leaf", "panel", None, None),
        P("leaf", "panel", None),
        P("leaf", "panel"),
    )
    out_specs = (P("leaf", "panel", None, None), P("leaf", "panel", None, None))
    return jax.shard_map(body, mesh=mesh, in_specs=in_specs, out_specs=out_specs, check_vma=False)
```

```python
import jax
import jax.numpy as jnp
from jax import lax
from jax.sharding import PartitionSpec as P
from jax.experimental.layout import Layout, with_layout_constraint

CHUNKS = 4


def shift_leaf(block, pairs):
    return lax.ppermute(block, "leaf", pairs)


def exchange(buffer):
    return lax.all_to_all(buffer, "panel", split_axis=0, concat_axis=0, tiled=True)


def split3(a):
    rounded = lambda v: lax.reduce_precision(v, exponent_bits=8, mantissa_bits=7)
    hi = rounded(a)
    rest = a - hi
    mid = rounded(rest)
    lo = rest - mid
    return tuple(p.astype(jnp.bfloat16) for p in (hi, mid, lo))


def product(x, parts):
    hi, mid, lo = parts
    rows = x.shape[1]
    xh, xm, xl = split3(x)
    mul = lambda a, w: jnp.einsum("nrw,nwv->nrv", a, w, preferred_element_type=jnp.float32)
    first = mul(jnp.concatenate([xh, xm, xl], axis=1), hi)
    second = mul(jnp.concatenate([xh, xm], axis=1), mid)
    third = mul(xh, lo)
    small = (first[:, 2 * rows:] + second[:, rows:] + third) + (first[:, rows:2 * rows] + second[:, :rows])
    return small + first[:, :rows]


def apply(x, matrix, parts, early):
    if early:
        return jnp.einsum("nrw,nwv->nrv", x, matrix, precision=lax.Precision.HIGHEST)
    return product(x, parts)


def pick_chunk(chunks, index):
    out = chunks[0]
    for j in range(1, len(chunks)):
        out = jnp.where(index == j, chunks[j], out)
    return out


def store_chunk(chunks, index, piece):
    return [jnp.where(index == j, piece, c) for j, c in enumerate(chunks)]


def body(right_sides, inverse, coupling, owner_map, parent_slot):
    highest = lax.Precision.HIGHEST
    levels = lax.axis_size("leaf")
    panels = lax.axis_size("panel")
    level = lax.axis_index("leaf")
    node_count = right_sides.shape[1]
    total_cols = right_sides.shape[2]
    width = right_sides.shape[3]
    capacity = max(2, 2 * node_count // panels)
    slot_count = panels * capacity
    owners = owner_map[0, :, 0]
    positions = parent_slot[0]
    node_iota = jnp.arange(node_count, dtype=jnp.int32)
    same_owner = owners[:, None] == owners[None, :]
    before = node_iota[None, :] < node_iota[:, None]
    slot_rank = jnp.sum((same_owner & before).astype(jnp.int32), axis=1)
    dest_slot = owners * capacity + slot_rank
    slot_iota = jnp.arange(slot_count, dtype=jnp.int32)
    send_onehot = (slot_iota[:, None] == dest_slot[None, :]).astype(jnp.float32)
    send_ids = jnp.dot(send_onehot, (positions + 1).astype(jnp.float32), precision=highest) - 1.0
    arrived_ids = exchange(send_ids)
    node_float = node_iota.astype(jnp.float32)
    recv_onehot = (arrived_ids[None, :] == node_float[:, None]).astype(jnp.float32)

    chunks = CHUNKS
    rows = total_cols // chunks
    given = [right_sides[0, :, j * rows:(j + 1) * rows] for j in range(chunks)]
    diag_inverse = inverse[0]
    couple_block = coupling[0]
    row_major = Layout(major_to_minor=(0, 1, 2))
    inverse_t = with_layout_constraint(jnp.swapaxes(diag_inverse, 1, 2), row_major)
    couple_t = with_layout_constraint(jnp.swapaxes(couple_block, 1, 2), row_major)
    inverse_parts = split3(diag_inverse)
    couple_parts = split3(couple_block)
    inverse_t_parts = split3(inverse_t)
    couple_t_parts = split3(couple_t)
    zero_chunk = jnp.zeros((node_count, rows, width), jnp.float32)
    solved = [zero_chunk] * chunks
    result = [zero_chunk] * chunks
    incoming = zero_chunk
    picked = zero_chunk
    top = levels - 1
    turns = 2 * top + chunks
    for turn in range(turns):
        fwd_levels = [l for l in range(levels) if 0 <= turn - l < chunks]
        bwd_levels = [l for l in range(levels) if 0 <= turn - 2 * top + l < chunks]
        if fwd_levels:
            f_index = turn - level
            f_active = (f_index >= 0) & (f_index < chunks)
            rhs = pick_chunk(given, f_index)
            forward_part = apply(rhs - incoming, diag_inverse, inverse_parts, turn == 0)
            solved = store_chunk(solved, jnp.where(f_active, f_index, -1), forward_part)
        if bwd_levels:
            b_index = turn - 2 * top + level
            b_active = (b_index >= 0) & (b_index < chunks)
            source = pick_chunk(solved, b_index)
            if any(l < top for l in bwd_levels):
                lowered = apply(picked, couple_t, couple_t_parts, turn == top + 1)
                source = source - lowered
            backward_part = apply(source, inverse_t, inverse_t_parts, turn == top)
            result = store_chunk(result, jnp.where(b_active, b_index, -1), backward_part)
        senders = [l for l in fwd_levels if l < top]
        down = [l for l in bwd_levels if l > 0]
        if senders:
            updates = apply(forward_part, couple_block, couple_parts, turn == 0)
            fwd_buffer = jnp.einsum("ts,srw->trw", send_onehot, updates, precision=highest)
        if down:
            lowered_in = shift_leaf(backward_part, [(l, l - 1) for l in down])
            bwd_buffer = jnp.einsum("st,srw->trw", recv_onehot, lowered_in, precision=highest)
        if senders and down:
            arrived = exchange(jnp.concatenate([fwd_buffer, bwd_buffer], axis=1))
            fwd_arrived, bwd_arrived = arrived[:, :rows], arrived[:, rows:]
        elif senders:
            fwd_arrived = exchange(fwd_buffer)
        elif down:
            bwd_arrived = exchange(bwd_buffer)
        if senders:
            summed = jnp.einsum("st,trw->srw", recv_onehot, fwd_arrived, precision=highest)
            incoming = shift_leaf(summed, [(l, l + 1) for l in senders])
        else:
            incoming = zero_chunk
        if down:
            picked = jnp.einsum("ts,trw->srw", send_onehot, bwd_arrived, precision=highest)
        else:
            picked = zero_chunk
    solved_all = jnp.concatenate(solved, axis=1)
    result_all = jnp.concatenate(result, axis=1)
    return (solved_all[None], result_all[None])


def solution(mesh):
    in_specs = (
        P("leaf", "panel", None, None),
        P("leaf", "panel", None, None),
        P("leaf", "panel", None, None),
        P("leaf", "panel", None),
        P("leaf", "panel"),
    )
    out_specs = (P("leaf", "panel", None, None), P("leaf", "panel", None, None))
    return jax.shard_map(body, mesh=mesh, in_specs=in_specs, out_specs=out_specs, check_vma=False)
```

```python
import jax
import jax.numpy as jnp
from jax import lax
from jax.sharding import PartitionSpec as P
from jax.experimental.layout import Layout, with_layout_constraint

CHUNKS = 4
MAIN_PRECISION = lax.Precision.HIGHEST


def shift_leaf(block, pairs):
    return lax.ppermute(block, "leaf", pairs)


def exchange(buffer):
    return lax.all_to_all(buffer, "panel", split_axis=0, concat_axis=0, tiled=True)


def pick_chunk(chunks, index):
    out = chunks[0]
    for j in range(1, len(chunks)):
        out = jnp.where(index == j, chunks[j], out)
    return out


def store_chunk(chunks, index, piece):
    return [jnp.where(index == j, piece, c) for j, c in enumerate(chunks)]


def body(right_sides, inverse, coupling, owner_map, parent_slot):
    highest = lax.Precision.HIGHEST
    main = MAIN_PRECISION
    levels = lax.axis_size("leaf")
    panels = lax.axis_size("panel")
    level = lax.axis_index("leaf")
    node_count = right_sides.shape[1]
    total_cols = right_sides.shape[2]
    width = right_sides.shape[3]
    capacity = max(2, 2 * node_count // panels)
    slot_count = panels * capacity
    owners = owner_map[0, :, 0]
    positions = parent_slot[0]
    node_iota = jnp.arange(node_count, dtype=jnp.int32)
    same_owner = owners[:, None] == owners[None, :]
    before = node_iota[None, :] < node_iota[:, None]
    slot_rank = jnp.sum((same_owner & before).astype(jnp.int32), axis=1)
    dest_slot = owners * capacity + slot_rank
    slot_iota = jnp.arange(slot_count, dtype=jnp.int32)
    send_onehot = (slot_iota[:, None] == dest_slot[None, :]).astype(jnp.float32)
    send_ids = jnp.dot(send_onehot, (positions + 1).astype(jnp.float32), precision=highest) - 1.0
    arrived_ids = exchange(send_ids)
    node_float = node_iota.astype(jnp.float32)
    recv_onehot = (arrived_ids[None, :] == node_float[:, None]).astype(jnp.float32)

    chunks = CHUNKS
    rows = total_cols // chunks
    given = [right_sides[0, :, j * rows:(j + 1) * rows] for j in range(chunks)]
    diag_inverse = inverse[0]
    couple_block = coupling[0]
    row_major = Layout(major_to_minor=(0, 1, 2))
    inverse_t = with_layout_constraint(jnp.swapaxes(diag_inverse, 1, 2), row_major)
    couple_t = with_layout_constraint(jnp.swapaxes(couple_block, 1, 2), row_major)
    zero_chunk = jnp.zeros((node_count, rows, width), jnp.float32)
    solved = [zero_chunk] * chunks
    result = [zero_chunk] * chunks
    incoming = zero_chunk
    picked = zero_chunk
    top = levels - 1
    turns = 2 * top + chunks
    for turn in range(turns):
        fwd_levels = [l for l in range(levels) if 0 <= turn - l < chunks]
        bwd_levels = [l for l in range(levels) if 0 <= turn - 2 * top + l < chunks]
        if fwd_levels:
            f_index = turn - level
            f_active = (f_index >= 0) & (f_index < chunks)
            rhs = pick_chunk(given, f_index)
            forward_part = jnp.einsum("nrw,nwv->nrv", rhs - incoming, diag_inverse, precision=main)
            solved = store_chunk(solved, jnp.where(f_active, f_index, -1), forward_part)
        if bwd_levels:
            b_index = turn - 2 * top + level
            b_active = (b_index >= 0) & (b_index < chunks)
            source = pick_chunk(solved, b_index)
            if any(l < top for l in bwd_levels):
                lowered = jnp.einsum("nrv,nvw->nrw", picked, couple_t, precision=main)
                source = source - lowered
            backward_part = jnp.einsum("nrw,nwv->nrv", source, inverse_t, precision=main)
            result = store_chunk(result, jnp.where(b_active, b_index, -1), backward_part)
        senders = [l for l in fwd_levels if l < top]
        down = [l for l in bwd_levels if l > 0]
        if senders:
            updates = jnp.einsum("nrw,nwv->nrv", forward_part, couple_block, precision=main)
            fwd_buffer = jnp.einsum("ts,srw->trw", send_onehot, updates, precision=highest)
        if down:
            lowered_in = shift_leaf(backward_part, [(l, l - 1) for l in down])
            bwd_buffer = jnp.einsum("st,srw->trw", recv_onehot, lowered_in, precision=highest)
        if senders and down:
            arrived = exchange(jnp.concatenate([fwd_buffer, bwd_buffer], axis=1))
            fwd_arrived, bwd_arrived = arrived[:, :rows], arrived[:, rows:]
        elif senders:
            fwd_arrived = exchange(fwd_buffer)
        elif down:
            bwd_arrived = exchange(bwd_buffer)
        if senders:
            summed = jnp.einsum("st,trw->srw", recv_onehot, fwd_arrived, precision=highest)
            incoming = shift_leaf(summed, [(l, l + 1) for l in senders])
            if turn == 0:
                incoming, inverse_t, couple_t = lax.optimization_barrier((incoming, inverse_t, couple_t))
        else:
            incoming = zero_chunk
        if down:
            picked = jnp.einsum("ts,trw->srw", send_onehot, bwd_arrived, precision=highest)
        else:
            picked = zero_chunk
    solved_all = jnp.concatenate(solved, axis=1)
    result_all = jnp.concatenate(result, axis=1)
    return (solved_all[None], result_all[None])


def solution(mesh):
    in_specs = (
        P("leaf", "panel", None, None),
        P("leaf", "panel", None, None),
        P("leaf", "panel", None, None),
        P("leaf", "panel", None),
        P("leaf", "panel"),
    )
    out_specs = (P("leaf", "panel", None, None), P("leaf", "panel", None, None))
    return jax.shard_map(body, mesh=mesh, in_specs=in_specs, out_specs=out_specs, check_vma=False)
```

```python
import jax
import jax.numpy as jnp
from jax import lax
from jax.sharding import PartitionSpec as P
from jax.experimental.layout import Layout, with_layout_constraint

CHUNKS = 4
MAIN_PRECISION = lax.Precision.HIGHEST


def shift_leaf(block, pairs):
    return lax.ppermute(block, "leaf", pairs)


def exchange(buffer):
    return lax.all_to_all(buffer, "panel", split_axis=0, concat_axis=0, tiled=True)


def pick_chunk(chunks, index):
    out = chunks[0]
    for j in range(1, len(chunks)):
        out = jnp.where(index == j, chunks[j], out)
    return out


def store_chunk(chunks, index, piece):
    return [jnp.where(index == j, piece, c) for j, c in enumerate(chunks)]


def body(right_sides, inverse, coupling, owner_map, parent_slot):
    highest = lax.Precision.HIGHEST
    main = MAIN_PRECISION
    levels = lax.axis_size("leaf")
    panels = lax.axis_size("panel")
    level = lax.axis_index("leaf")
    node_count = right_sides.shape[1]
    total_cols = right_sides.shape[2]
    width = right_sides.shape[3]
    capacity = max(2, 2 * node_count // panels)
    slot_count = panels * capacity
    owners = owner_map[0, :, 0]
    positions = parent_slot[0]
    node_iota = jnp.arange(node_count, dtype=jnp.int32)
    same_owner = owners[:, None] == owners[None, :]
    before = node_iota[None, :] < node_iota[:, None]
    slot_rank = jnp.sum((same_owner & before).astype(jnp.int32), axis=1)
    dest_slot = owners * capacity + slot_rank
    slot_iota = jnp.arange(slot_count, dtype=jnp.int32)
    send_onehot = (slot_iota[:, None] == dest_slot[None, :]).astype(jnp.float32)
    send_ids = jnp.dot(send_onehot, (positions + 1).astype(jnp.float32), precision=highest) - 1.0
    arrived_ids = exchange(send_ids)
    node_float = node_iota.astype(jnp.float32)
    recv_onehot = (arrived_ids[None, :] == node_float[:, None]).astype(jnp.float32)

    chunks = CHUNKS
    rows = total_cols // chunks
    given = [right_sides[0, :, j * rows:(j + 1) * rows] for j in range(chunks)]
    diag_inverse = inverse[0]
    couple_block = coupling[0]
    row_major = Layout(major_to_minor=(0, 1, 2))
    inverse_t = with_layout_constraint(jnp.swapaxes(diag_inverse, 1, 2), row_major)
    couple_t = with_layout_constraint(jnp.swapaxes(couple_block, 1, 2), row_major)
    zero_chunk = jnp.zeros((node_count, rows, width), jnp.float32)
    solved = [zero_chunk] * chunks
    result = [zero_chunk] * chunks
    incoming = zero_chunk
    picked = zero_chunk
    top = levels - 1
    turns = 2 * top + chunks
    for turn in range(turns):
        fwd_levels = [l for l in range(levels) if 0 <= turn - l < chunks]
        bwd_levels = [l for l in range(levels) if 0 <= turn - 2 * top + l < chunks]
        if fwd_levels:
            f_index = turn - level
            f_active = (f_index >= 0) & (f_index < chunks)
            rhs = pick_chunk(given, f_index)
            forward_part = jnp.einsum("nrw,nwv->nrv", rhs - incoming, diag_inverse, precision=main)
            solved = store_chunk(solved, jnp.where(f_active, f_index, -1), forward_part)
        if bwd_levels:
            b_index = turn - 2 * top + level
            b_active = (b_index >= 0) & (b_index < chunks)
            source = pick_chunk(solved, b_index)
            if any(l < top for l in bwd_levels):
                lowered = jnp.einsum("nrv,nvw->nrw", picked, couple_t, precision=main)
                source = source - lowered
            backward_part = jnp.einsum("nrw,nwv->nrv", source, inverse_t, precision=main)
            result = store_chunk(result, jnp.where(b_active, b_index, -1), backward_part)
        senders = [l for l in fwd_levels if l < top]
        down = [l for l in bwd_levels if l > 0]
        if senders:
            updates = jnp.einsum("nrw,nwv->nrv", forward_part, couple_block, precision=main)
            fwd_buffer = jnp.einsum("ts,srw->trw", send_onehot, updates, precision=highest)
        if down:
            lowered_in = shift_leaf(backward_part, [(l, l - 1) for l in down])
            bwd_buffer = jnp.einsum("st,srw->trw", recv_onehot, lowered_in, precision=highest)
        if senders and down:
            arrived = exchange(jnp.concatenate([fwd_buffer, bwd_buffer], axis=1))
            fwd_arrived, bwd_arrived = arrived[:, :rows], arrived[:, rows:]
        elif senders:
            fwd_arrived = exchange(fwd_buffer)
            if turn == 0:
                fwd_arrived, inverse_t = lax.optimization_barrier((fwd_arrived, inverse_t))
        elif down:
            bwd_arrived = exchange(bwd_buffer)
        if senders:
            summed = jnp.einsum("st,trw->srw", recv_onehot, fwd_arrived, precision=highest)
            incoming = shift_leaf(summed, [(l, l + 1) for l in senders])
            if turn == 0:
                incoming, couple_t = lax.optimization_barrier((incoming, couple_t))
        else:
            incoming = zero_chunk
        if down:
            picked = jnp.einsum("ts,trw->srw", send_onehot, bwd_arrived, precision=highest)
        else:
            picked = zero_chunk
    solved_all = jnp.concatenate(solved, axis=1)
    result_all = jnp.concatenate(result, axis=1)
    return (solved_all[None], result_all[None])


def solution(mesh):
    in_specs = (
        P("leaf", "panel", None, None),
        P("leaf", "panel", None, None),
        P("leaf", "panel", None, None),
        P("leaf", "panel", None),
        P("leaf", "panel"),
    )
    out_specs = (P("leaf", "panel", None, None), P("leaf", "panel", None, None))
    return jax.shard_map(body, mesh=mesh, in_specs=in_specs, out_specs=out_specs, check_vma=False)
```

```python
import jax
import jax.numpy as jnp
from jax import lax
from jax.sharding import PartitionSpec as P
from jax.experimental.layout import Layout, with_layout_constraint

CHUNKS = 4
MAIN_PRECISION = lax.Precision.HIGHEST


def shift_leaf(block, pairs):
    return lax.ppermute(block, "leaf", pairs)


def exchange(buffer):
    return lax.all_to_all(buffer, "panel", split_axis=0, concat_axis=0, tiled=True)


def pick_chunk(chunks, index):
    out = chunks[0]
    for j in range(1, len(chunks)):
        out = jnp.where(index == j, chunks[j], out)
    return out


def store_chunk(chunks, index, piece):
    return [jnp.where(index == j, piece, c) for j, c in enumerate(chunks)]


def body(right_sides, inverse, coupling, owner_map, parent_slot):
    highest = lax.Precision.HIGHEST
    main = MAIN_PRECISION
    levels = lax.axis_size("leaf")
    panels = lax.axis_size("panel")
    level = lax.axis_index("leaf")
    node_count = right_sides.shape[1]
    total_cols = right_sides.shape[2]
    width = right_sides.shape[3]
    capacity = max(2, 2 * node_count // panels)
    slot_count = panels * capacity
    owners = owner_map[0, :, 0]
    positions = parent_slot[0]
    node_iota = jnp.arange(node_count, dtype=jnp.int32)
    same_owner = owners[:, None] == owners[None, :]
    before = node_iota[None, :] < node_iota[:, None]
    slot_rank = jnp.sum((same_owner & before).astype(jnp.int32), axis=1)
    dest_slot = owners * capacity + slot_rank
    slot_iota = jnp.arange(slot_count, dtype=jnp.int32)
    send_onehot = (slot_iota[:, None] == dest_slot[None, :]).astype(jnp.float32)
    send_ids = jnp.dot(send_onehot, (positions + 1).astype(jnp.float32), precision=highest) - 1.0
    node_float = node_iota.astype(jnp.float32)

    chunks = CHUNKS
    rows = total_cols // chunks
    given = [right_sides[0, :, j * rows:(j + 1) * rows] for j in range(chunks)]
    diag_inverse = inverse[0]
    couple_block = coupling[0]
    row_major = Layout(major_to_minor=(0, 1, 2))
    inverse_t = with_layout_constraint(jnp.swapaxes(diag_inverse, 1, 2), row_major)
    couple_t = with_layout_constraint(jnp.swapaxes(couple_block, 1, 2), row_major)
    zero_chunk = jnp.zeros((node_count, rows, width), jnp.float32)
    solved = [zero_chunk] * chunks
    result = [zero_chunk] * chunks
    incoming = zero_chunk
    picked = zero_chunk
    top = levels - 1
    turns = 2 * top + chunks
    for turn in range(turns):
        fwd_levels = [l for l in range(levels) if 0 <= turn - l < chunks]
        bwd_levels = [l for l in range(levels) if 0 <= turn - 2 * top + l < chunks]
        if fwd_levels:
            f_index = turn - level
            f_active = (f_index >= 0) & (f_index < chunks)
            rhs = pick_chunk(given, f_index)
            forward_part = jnp.einsum("nrw,nwv->nrv", rhs - incoming, diag_inverse, precision=main)
            solved = store_chunk(solved, jnp.where(f_active, f_index, -1), forward_part)
        if bwd_levels:
            b_index = turn - 2 * top + level
            b_active = (b_index >= 0) & (b_index < chunks)
            source = pick_chunk(solved, b_index)
            if any(l < top for l in bwd_levels):
                lowered = jnp.einsum("nrv,nvw->nrw", picked, couple_t, precision=main)
                source = source - lowered
            backward_part = jnp.einsum("nrw,nwv->nrv", source, inverse_t, precision=main)
            result = store_chunk(result, jnp.where(b_active, b_index, -1), backward_part)
        senders = [l for l in fwd_levels if l < top]
        down = [l for l in bwd_levels if l > 0]
        if senders:
            updates = jnp.einsum("nrw,nwv->nrv", forward_part, couple_block, precision=main)
            fwd_buffer = jnp.einsum("ts,srw->trw", send_onehot, updates, precision=highest)
        if down:
            lowered_in = shift_leaf(backward_part, [(l, l - 1) for l in down])
            bwd_buffer = jnp.einsum("st,srw->trw", recv_onehot, lowered_in, precision=highest)
        if senders and down:
            arrived = exchange(jnp.concatenate([fwd_buffer, bwd_buffer], axis=1))
            fwd_arrived, bwd_arrived = arrived[:, :rows], arrived[:, rows:]
        elif turn == 0:
            id_rows = jnp.broadcast_to(send_ids[:, None, None], (slot_count, 8, width))
            arrived = exchange(jnp.concatenate([fwd_buffer, id_rows], axis=1))
            fwd_arrived = arrived[:, :rows]
            recv_onehot = (arrived[:, rows, 0][None, :] == node_float[:, None]).astype(jnp.float32)
        elif senders:
            fwd_arrived = exchange(fwd_buffer)
        elif down:
            bwd_arrived = exchange(bwd_buffer)
        if senders:
            summed = jnp.einsum("st,trw->srw", recv_onehot, fwd_arrived, precision=highest)
            incoming = shift_leaf(summed, [(l, l + 1) for l in senders])
        else:
            incoming = zero_chunk
        if down:
            picked = jnp.einsum("ts,trw->srw", send_onehot, bwd_arrived, precision=highest)
        else:
            picked = zero_chunk
    solved_all = jnp.concatenate(solved, axis=1)
    result_all = jnp.concatenate(result, axis=1)
    return (solved_all[None], result_all[None])


def solution(mesh):
    in_specs = (
        P("leaf", "panel", None, None),
        P("leaf", "panel", None, None),
        P("leaf", "panel", None, None),
        P("leaf", "panel", None),
        P("leaf", "panel"),
    )
    out_specs = (P("leaf", "panel", None, None), P("leaf", "panel", None, None))
    return jax.shard_map(body, mesh=mesh, in_specs=in_specs, out_specs=out_specs, check_vma=False)
```

```python
import jax
import jax.numpy as jnp
from jax import lax
from jax.sharding import PartitionSpec as P
from jax.experimental.layout import Layout, with_layout_constraint

CHUNKS = 2
MAIN_PRECISION = lax.Precision.HIGHEST


def shift_leaf(block, pairs):
    return lax.ppermute(block, "leaf", pairs)


def exchange(buffer):
    return lax.all_to_all(buffer, "panel", split_axis=0, concat_axis=0, tiled=True)


def pick_chunk(chunks, index):
    out = chunks[0]
    for j in range(1, len(chunks)):
        out = jnp.where(index == j, chunks[j], out)
    return out


def store_chunk(chunks, index, piece):
    return [jnp.where(index == j, piece, c) for j, c in enumerate(chunks)]


def body(right_sides, inverse, coupling, owner_map, parent_slot):
    highest = lax.Precision.HIGHEST
    main = MAIN_PRECISION
    levels = lax.axis_size("leaf")
    panels = lax.axis_size("panel")
    level = lax.axis_index("leaf")
    node_count = right_sides.shape[1]
    total_cols = right_sides.shape[2]
    width = right_sides.shape[3]
    capacity = max(2, 2 * node_count // panels)
    slot_count = panels * capacity
    owners = owner_map[0, :, 0]
    positions = parent_slot[0]
    node_iota = jnp.arange(node_count, dtype=jnp.int32)
    same_owner = owners[:, None] == owners[None, :]
    before = node_iota[None, :] < node_iota[:, None]
    slot_rank = jnp.sum((same_owner & before).astype(jnp.int32), axis=1)
    dest_slot = owners * capacity + slot_rank
    slot_iota = jnp.arange(slot_count, dtype=jnp.int32)
    send_onehot = (slot_iota[:, None] == dest_slot[None, :]).astype(jnp.float32)
    send_ids = jnp.dot(send_onehot, (positions + 1).astype(jnp.float32), precision=highest) - 1.0
    node_float = node_iota.astype(jnp.float32)

    chunks = CHUNKS
    rows = total_cols // chunks
    given = [right_sides[0, :, j * rows:(j + 1) * rows] for j in range(chunks)]
    diag_inverse = inverse[0]
    couple_block = coupling[0]
    row_major = Layout(major_to_minor=(0, 1, 2))
    inverse_t = with_layout_constraint(jnp.swapaxes(diag_inverse, 1, 2), row_major)
    couple_t = with_layout_constraint(jnp.swapaxes(couple_block, 1, 2), row_major)
    zero_chunk = jnp.zeros((node_count, rows, width), jnp.float32)
    solved = [zero_chunk] * chunks
    result = [zero_chunk] * chunks
    incoming = zero_chunk
    picked = zero_chunk
    top = levels - 1
    turns = 2 * top + chunks
    for turn in range(turns):
        fwd_levels = [l for l in range(levels) if 0 <= turn - l < chunks]
        bwd_levels = [l for l in range(levels) if 0 <= turn - 2 * top + l < chunks]
        if fwd_levels:
            f_index = turn - level
            f_active = (f_index >= 0) & (f_index < chunks)
            rhs = pick_chunk(given, f_index)
            forward_part = jnp.einsum("nrw,nwv->nrv", rhs - incoming, diag_inverse, precision=main)
            solved = store_chunk(solved, jnp.where(f_active, f_index, -1), forward_part)
        if bwd_levels:
            b_index = turn - 2 * top + level
            b_active = (b_index >= 0) & (b_index < chunks)
            source = pick_chunk(solved, b_index)
            if any(l < top for l in bwd_levels):
                lowered = jnp.einsum("nrv,nvw->nrw", picked, couple_t, precision=main)
                source = source - lowered
            backward_part = jnp.einsum("nrw,nwv->nrv", source, inverse_t, precision=main)
            result = store_chunk(result, jnp.where(b_active, b_index, -1), backward_part)
        senders = [l for l in fwd_levels if l < top]
        down = [l for l in bwd_levels if l > 0]
        if senders:
            updates = jnp.einsum("nrw,nwv->nrv", forward_part, couple_block, precision=main)
            fwd_buffer = jnp.einsum("ts,srw->trw", send_onehot, updates, precision=highest)
        if down:
            lowered_in = shift_leaf(backward_part, [(l, l - 1) for l in down])
            bwd_buffer = jnp.einsum("st,srw->trw", recv_onehot, lowered_in, precision=highest)
        if senders and down:
            arrived = exchange(jnp.concatenate([fwd_buffer, bwd_buffer], axis=1))
            fwd_arrived, bwd_arrived = arrived[:, :rows], arrived[:, rows:]
        elif turn == 0:
            id_rows = jnp.broadcast_to(send_ids[:, None, None], (slot_count, 8, width))
            arrived = exchange(jnp.concatenate([fwd_buffer, id_rows], axis=1))
            fwd_arrived = arrived[:, :rows]
            recv_onehot = (arrived[:, rows, 0][None, :] == node_float[:, None]).astype(jnp.float32)
        elif senders:
            fwd_arrived = exchange(fwd_buffer)
        elif down:
            bwd_arrived = exchange(bwd_buffer)
        if senders:
            summed = jnp.einsum("st,trw->srw", recv_onehot, fwd_arrived, precision=highest)
            incoming = shift_leaf(summed, [(l, l + 1) for l in senders])
        else:
            incoming = zero_chunk
        if down:
            picked = jnp.einsum("ts,trw->srw", send_onehot, bwd_arrived, precision=highest)
        else:
            picked = zero_chunk
    solved_all = jnp.concatenate(solved, axis=1)
    result_all = jnp.concatenate(result, axis=1)
    return (solved_all[None], result_all[None])


def solution(mesh):
    in_specs = (
        P("leaf", "panel", None, None),
        P("leaf", "panel", None, None),
        P("leaf", "panel", None, None),
        P("leaf", "panel", None),
        P("leaf", "panel"),
    )
    out_specs = (P("leaf", "panel", None, None), P("leaf", "panel", None, None))
    return jax.shard_map(body, mesh=mesh, in_specs=in_specs, out_specs=out_specs, check_vma=False)
```
